512 devices in a mesh: space: 128 (over z, y, core), mode: 4 (over x).
Axes of the slice: x: 4, y: 8, z: 8, core: 2. Of those that a mesh axis runs over, the one named last changes fastest.
Arguments:
- iterate: float32 [84, 16, 98304], P('mode', None, 'space'), may hold values from -6 to 6
- forcing: float32 [84, 16, 98304], P('mode', None, 'space'), may hold values from -6 to 6
- tiles: bfloat16 [3, 512, 3, 36864], P(None, 'space'), may hold values from -0.25 to 0.25
- inverse_blocks: bfloat16 [512, 36864], P('space'), may hold values from -0.4375 to 0.4375
- columns: int32 [512, 3], P('space'), may hold values from 0 to 7, as said below
- coupling: float32 [3, 84, 84], replicated, may hold values from -0.7 to 1.5, as said below
Outputs:
- updated: float32 [84, 16, 98304], P('mode', None, 'space')
- residual: float32 [84, 16, 98304], P('mode', None, 'space')
The draws below stay inside these ranges and needn't reach their ends.
Inputs may be any that keep to these rules, and one draw needn't show every extreme that they name: For row block j at position q = j mod 4 of its device: columns[j, 0] = 2 + q; columns[j, 1] = 2 + q - 1 or 2 + q - 2; columns[j, 2] = 2 + q + 1 or 2 + q + 2. At q = 0 slot 1 is 2 + q - 2, at q = 3 slot 2 is 2 + q + 2. `coupling`: each matrix is symmetric; the first has ones added on its diagonal.
All inputs are finite; a program needn't handle non-finite values.
Results may differ from the reference program's by a relative error of at most 0.0033.
Values may be sent and summed in bfloat16 or wider, within the bound.
No kernel may reach another device: no remote copies, remote signals or barrier semaphores. Data moves between devices by JAX's collectives and lax.ppermute only.
A program may use at most 64 MiB of HBM per device.

```python
import jax
import jax.numpy as jnp
from jax import lax

P_SIZE = 84
BS = 192
KL = 3
S = 3
H = 2
B_LOC = 4
LOADS = 16
NB = 512
NDOF = 98304


def draw_columns(key, part):
    position = jnp.arange(NB, dtype=jnp.int32) % B_LOC
    reach = jax.random.randint(key, (NB, 2), 1, 3, dtype=jnp.int32)
    behind = jnp.where(position == 0, 2, reach[:, 0])
    ahead = jnp.where(position == B_LOC - 1, 2, reach[:, 1])
    stacked = jnp.stack([H + position, H + position - behind, H + position + ahead], axis=1)
    return stacked.astype(jnp.int32)


def draw_coupling(key, part):
    first_key, second_key = jax.random.split(key)
    raw_values = jnp.clip(jax.random.normal(first_key, (KL, P_SIZE, P_SIZE), jnp.float32), -4.0, 4.0)
    pattern = jax.random.uniform(second_key, (KL, P_SIZE, P_SIZE), jnp.float32)
    pattern = pattern + jnp.swapaxes(pattern, 1, 2)
    kept = jnp.where(pattern < 0.7, 1.0, 0.0)
    values = (raw_values + jnp.swapaxes(raw_values, 1, 2)) * 0.7071 * kept
    scales = jnp.where(jnp.arange(KL) == 0, 0.08, 0.12)[:, None, None]
    diagonal = jnp.where(jnp.arange(P_SIZE)[:, None] == jnp.arange(P_SIZE)[None, :], 1.0, 0.0)
    first_term = jnp.where(jnp.arange(KL) == 0, 1.0, 0.0)[:, None, None]
    return (values * scales + first_term * diagonal[None]).astype(jnp.float32)


def block_levels(stream_key, extent, pieces, low, high):
    def one(axis_at, shards_of):
        heights = jax.random.uniform(jax.random.fold_in(jax.random.fold_in(stream_key, 6), axis_at), (shards_of,), jnp.float32, low / len(pieces), high / len(pieces))
        return jnp.repeat(jnp.exp(heights), extent[axis_at] // shards_of).reshape((-1,) + (1,) * (len(extent) - axis_at - 1))

    loudness = one(*pieces[0])
    for cut in pieces[1:]:
        loudness = loudness * one(*cut)
    return loudness


def bell_draw(rng, shape, width, most, cuts=(), kind=jnp.bfloat16):
    drawn = jax.random.normal(rng, shape, jnp.float32) * width
    if len(cuts) > 0:
        drawn = block_levels(rng, shape, cuts, -0.22, 0.18) * drawn
    return jnp.clip(drawn, min=-most, max=most).astype(kind)


def setup_inputs(seed: int = 0) -> dict:
    splits = jax.random.split(jax.random.key(seed), 7)
    iterate = bell_draw(splits[0], (P_SIZE, LOADS, NDOF), 1.0, 6.0, ((0, 4), (2, 128)), jnp.float32)
    forcing = bell_draw(splits[1], (P_SIZE, LOADS, NDOF), 1.0, 6.0, ((0, 4), (2, 128)), jnp.float32)
    tiles = bell_draw(splits[2], (KL, NB, S, BS * BS), (S * BS) ** -0.5, 0.25, ((1, 128),))
    inverse_blocks = bell_draw(splits[3], (NB, BS * BS), BS ** -0.5, 0.4375, ((0, 128),))
    columns = draw_columns(jax.random.fold_in(splits[6], 71), 0)
    coupling = draw_coupling(jax.random.fold_in(splits[6], 71), 0)
    return {"iterate": iterate, "forcing": forcing, "tiles": tiles, "inverse_blocks": inverse_blocks, "columns": columns, "coupling": coupling}


RELAXATION = 0.7


def reference(iterate, forcing, tiles, inverse_blocks, columns, coupling):
    rounded = iterate.astype(jnp.bfloat16)
    rounded = lax.optimization_barrier(rounded).astype(jnp.float32).reshape(P_SIZE, LOADS, NB, BS)
    blocks = jnp.arange(NB, dtype=jnp.int32)
    anchor = (blocks // B_LOC) * B_LOC - H
    target = ((anchor[:, None] + columns.astype(jnp.int32)) % NB).astype(jnp.int32)
    picked = rounded[:, :, target, :]

    def one_term(tile_term):
        shaped = tile_term.astype(jnp.float32).reshape(NB, S, BS, BS)
        return jnp.einsum("rsim,plrsm->plri", shaped, picked).astype(jnp.bfloat16)

    products = lax.map(one_term, tiles)
    products = lax.optimization_barrier(products)
    flat = products.astype(jnp.float32).reshape(KL, P_SIZE, LOADS, NB * BS)
    applied = jnp.einsum("kab,kbln->aln", coupling, flat, precision=lax.Precision.HIGHEST)
    residual = forcing - applied
    rounded_res = lax.optimization_barrier(residual.astype(jnp.bfloat16))
    rounded_res = rounded_res.astype(jnp.float32).reshape(P_SIZE, LOADS, NB, BS)
    inverse = inverse_blocks.astype(jnp.float32).reshape(NB, BS, BS)
    update = jnp.einsum("jim,pljm->plji", inverse, rounded_res).reshape(P_SIZE, LOADS, NB * BS)
    updated = iterate + RELAXATION * update
    return updated, residual
```

```python
import functools

import jax
import jax.numpy as jnp
from jax import lax
from jax.experimental import pallas as pl
from jax.experimental.pallas import tpu as pltpu
from jax.sharding import PartitionSpec as P

H = 2


RELAXATION = 0.7


def halos(x, axis, width):
    devices = lax.axis_size(axis)
    blocks = x.shape[1]
    up = [(i, (i + 1) % devices) for i in range(devices)]
    down = [(j, i) for i, j in up]
    left = lax.ppermute(x[:, blocks - width:], axis, up)
    right = lax.ppermute(x[:, :width], axis, down)
    return left, right


def stiffness_kernel(cols_ref, xl_ref, xc_ref, xr_ref, t_ref, o_ref, acc_ref):
    r = pl.program_id(0)
    slots = t_ref.shape[2]
    width = xl_ref.shape[1]
    blocks = xc_ref.shape[1]
    block_size = t_ref.shape[-1]
    acc_ref[...] = jnp.zeros_like(acc_ref)

    def add_block(src_ref, idx, tile):
        xs = src_ref[:, idx]
        xs = xs.reshape(-1, block_size)
        acc_ref[...] += lax.dot_general(
            xs, tile, (((1,), (1,)), ((), ())), preferred_element_type=jnp.float32
        )

    for s in range(slots):
        e = cols_ref[r * slots + s]
        tile = t_ref[0, 0, s]

        @pl.when(e < width)
        def _():
            add_block(xl_ref, jnp.clip(e, 0, width - 1), tile)

        @pl.when((e >= width) & (e < width + blocks))
        def _():
            add_block(xc_ref, jnp.clip(e - width, 0, blocks - 1), tile)

        @pl.when(e >= width + blocks)
        def _():
            add_block(xr_ref, jnp.clip(e - width - blocks, 0, width - 1), tile)

    o_ref[0, 0] = acc_ref[...].reshape(o_ref.shape[2:]).astype(o_ref.dtype)


def stiffness(cols, xl, xc, xr, tiles5):
    terms, blocks, slots, bs, _ = tiles5.shape
    nm, _, rows, _ = xc.shape
    width = xl.shape[1]
    full = lambda r, k, c: (0, 0, 0, 0)
    return pl.pallas_call(
        stiffness_kernel,
        out_shape=jax.ShapeDtypeStruct((terms, blocks, nm, rows, bs), jnp.bfloat16),
        grid_spec=pltpu.PrefetchScalarGridSpec(
            num_scalar_prefetch=1,
            grid=(blocks, terms),
            in_specs=[
                pl.BlockSpec((nm, width, rows, bs), full),
                pl.BlockSpec((nm, blocks, rows, bs), full),
                pl.BlockSpec((nm, width, rows, bs), full),
                pl.BlockSpec((1, 1, slots, bs, bs), lambda r, k, c: (k, r, 0, 0, 0)),
            ],
            out_specs=pl.BlockSpec((1, 1, nm, rows, bs), lambda r, k, c: (k, r, 0, 0, 0)),
            scratch_shapes=[pltpu.VMEM((nm * rows, bs), jnp.float32)],
        ),
        compiler_params=pltpu.CompilerParams(vmem_limit_bytes=60 * 1024 * 1024),
        cost_estimate=pl.CostEstimate(
            flops=2 * terms * blocks * slots * nm * rows * bs * bs,
            transcendentals=0,
            bytes_accessed=2 * (tiles5.size + xc.size + xl.size + xr.size + terms * blocks * nm * rows * bs),
        ),
    )(cols, xl, xc, xr, tiles5)


def body(iterate, forcing, tiles, inverse_blocks, columns, coupling):
    modes_here, loads, dofs_here = iterate.shape
    terms, block_count, slots = tiles.shape[:3]
    block_size = dofs_here // block_count
    nm = lax.axis_size("mode")
    rounded = iterate.astype(jnp.bfloat16).reshape(modes_here, loads, block_count, block_size)
    rounded = jnp.transpose(rounded, (2, 0, 1, 3)).reshape(block_count, modes_here * loads, block_size)
    gathered = lax.all_gather(rounded, "mode", axis=0, tiled=False)
    left, right = halos(gathered, "space", H)
    tiles5 = tiles.reshape(terms, block_count, slots, block_size, block_size)
    cols = columns.reshape(-1).astype(jnp.int32)
    products = stiffness(cols, left, gathered, right, tiles5)
    products = products.reshape(terms, block_count, nm, modes_here, loads, block_size)
    first = lax.axis_index("mode") * modes_here
    mine = lax.dynamic_slice_in_dim(coupling, first, modes_here, axis=1)
    mine = mine.reshape(terms, modes_here, nm, modes_here)
    mixture = jnp.einsum(
        "kamp,krmpli->alri",
        mine,
        products.astype(jnp.float32),
        precision=lax.Precision.HIGHEST,
    )
    applied = mixture.reshape(modes_here, loads, dofs_here)
    residual = forcing - applied
    rounded_res = residual.astype(jnp.bfloat16).reshape(modes_here, loads, block_count, block_size)
    inverse = inverse_blocks.reshape(block_count, block_size, block_size)
    update = jnp.einsum("jim,pljm->plji", inverse, rounded_res, preferred_element_type=jnp.float32)
    updated = iterate + RELAXATION * update.reshape(modes_here, loads, dofs_here)
    return (updated, residual)


def solution(mesh):
    return jax.shard_map(
        body,
        mesh=mesh,
        in_specs=(
            P("mode", None, "space"),
            P("mode", None, "space"),
            P(None, "space", None, None),
            P("space", None),
            P("space", None),
            P(),
        ),
        out_specs=(P("mode", None, "space"), P("mode", None, "space")),
        check_vma=False,
    )
```

```python
import jax
import jax.numpy as jnp
from jax import lax
from jax.experimental import pallas as pl
from jax.experimental.pallas import tpu as pltpu
from jax.sharding import PartitionSpec as P

H = 2


RELAXATION = 0.7


def shift(x, axis, k):
    devices = lax.axis_size(axis)
    return lax.ppermute(x, axis, [(i, (i + k) % devices) for i in range(devices)])


def extend(group, left, right):
    return jnp.concatenate([left, group, right], axis=-3)


def stiffness_kernel(cols_ref, x0_ref, x1_ref, x2_ref, t_ref, o_ref):
    nm = x0_ref.shape[0]
    modes_here = o_ref.shape[0] // nm
    loads, block_size = o_ref.shape[1:]
    for m in range(nm):
        acc = None
        for s, x_ref in enumerate((x0_ref, x1_ref, x2_ref)):
            d = lax.dot_general(
                x_ref[m], t_ref[s], (((1,), (1,)), ((), ())), preferred_element_type=jnp.float32
            )
            acc = d if acc is None else acc + d
        o_ref[m * modes_here:(m + 1) * modes_here] = (
            acc.astype(o_ref.dtype).reshape(modes_here, loads, block_size)
        )


def stiffness(cols, ext, tiles5, loads):
    terms, blocks, slots, bs, _ = tiles5.shape
    nm, _, rows, _ = ext.shape
    modes_all = nm * rows // loads

    def x_spec(s):
        return pl.BlockSpec((nm, None, rows, bs), lambda r, k, c: (0, c[r * slots + s], 0, 0))

    return pl.pallas_call(
        stiffness_kernel,
        out_shape=jax.ShapeDtypeStruct((terms, modes_all, blocks, loads, bs), jnp.bfloat16),
        grid_spec=pltpu.PrefetchScalarGridSpec(
            num_scalar_prefetch=1,
            grid=(blocks, terms),
            in_specs=[x_spec(s) for s in range(slots)]
            + [pl.BlockSpec((None, None, slots, bs, bs), lambda r, k, c: (k, r, 0, 0, 0))],
            out_specs=pl.BlockSpec(
                (None, modes_all, None, loads, bs), lambda r, k, c: (k, 0, r, 0, 0)
            ),
        ),
        compiler_params=pltpu.CompilerParams(vmem_limit_bytes=48 * 1024 * 1024),
        cost_estimate=pl.CostEstimate(
            flops=2 * terms * blocks * slots * nm * rows * bs * bs,
            transcendentals=0,
            bytes_accessed=2 * (tiles5.size + blocks * slots * nm * rows * bs + terms * blocks * nm * rows * bs),
        ),
    )(cols, ext, ext, ext, tiles5)


def body(iterate, forcing, tiles, inverse_blocks, columns, coupling):
    modes_here, loads, dofs_here = iterate.shape
    terms, block_count, slots = tiles.shape[:3]
    block_size = dofs_here // block_count
    nm = lax.axis_size("mode")
    me = lax.axis_index("mode")
    tiles5 = tiles.reshape(terms, block_count, slots, block_size, block_size)
    cols = columns.reshape(-1).astype(jnp.int32)
    rounded = iterate.astype(jnp.bfloat16).reshape(modes_here, loads, block_count, block_size)
    own = jnp.transpose(rounded, (2, 0, 1, 3)).reshape(block_count, modes_here * loads, block_size)
    low, high = own[:H], own[block_count - H:]
    from_left = shift(own, "mode", 1)
    from_right = shift(own, "mode", -1)
    near = jnp.stack([from_left, from_right])
    far_low = shift(from_left[:H], "mode", 1)
    far_high = shift(from_right[block_count - H:], "mode", -1)
    far = jnp.concatenate([far_low, far_high], axis=0)
    own_ext = extend(own, shift(high, "space", 1), shift(low, "space", -1))[None]
    near_ext = extend(
        near, shift(near[:, block_count - H:], "space", 1), shift(near[:, :H], "space", -1)
    )
    far_ext = extend(far, shift(far_high, "space", 1), shift(far_low, "space", -1))[None]
    rows_of = lax.dynamic_slice_in_dim(coupling, me * modes_here, modes_here, axis=1)

    def columns_of(index):
        return lax.dynamic_slice_in_dim(rows_of, (index % nm) * modes_here, modes_here, axis=2)

    parts = (
        (own_ext, columns_of(me)),
        (near_ext, jnp.concatenate([columns_of(me + nm - 1), columns_of(me + 1)], axis=2)),
        (far_ext, columns_of(me + 2)),
    )
    mixture = None
    for ext, mix in parts:
        products = stiffness(cols, ext, tiles5, loads)
        term = jnp.einsum(
            "kab,kbrli->alri", mix, products.astype(jnp.float32), precision=lax.Precision.HIGHEST
        )
        mixture = term if mixture is None else mixture + term
    applied = mixture.reshape(modes_here, loads, dofs_here)
    residual = forcing - applied
    rounded_res = residual.astype(jnp.bfloat16).reshape(modes_here, loads, block_count, block_size)
    inverse = inverse_blocks.reshape(block_count, block_size, block_size)
    update = jnp.einsum("jim,pljm->plji", inverse, rounded_res, preferred_element_type=jnp.float32)
    updated = iterate + RELAXATION * update.reshape(modes_here, loads, dofs_here)
    return (updated, residual)


def solution(mesh):
    return jax.shard_map(
        body,
        mesh=mesh,
        in_specs=(
            P("mode", None, "space"),
            P("mode", None, "space"),
            P(None, "space", None, None),
            P("space", None),
            P("space", None),
            P(),
        ),
        out_specs=(P("mode", None, "space"), P("mode", None, "space")),
        check_vma=False,
    )
```

```python
import jax
import jax.numpy as jnp
from jax import lax
from jax.experimental import pallas as pl
from jax.experimental.pallas import tpu as pltpu
from jax.sharding import PartitionSpec as P

H = 2


RELAXATION = 0.7


def shift(x, axis, k):
    devices = lax.axis_size(axis)
    return lax.ppermute(x, axis, [(i, (i + k) % devices) for i in range(devices)])


def stiffness_kernel(cols_ref, x0_ref, x1_ref, x2_ref, t_ref, o_ref):
    acc = None
    for s, x_ref in enumerate((x0_ref, x1_ref, x2_ref)):
        d = jnp.dot(x_ref[...], t_ref[s], preferred_element_type=jnp.float32)
        acc = d if acc is None else acc + d
    o_ref[...] = acc.astype(o_ref.dtype)


def stiffness(cols, ext, tiles_t, term):
    _, blocks, slots, bs, _ = tiles_t.shape
    _, rows, _ = ext.shape

    def x_spec(s):
        return pl.BlockSpec((None, rows, bs), lambda r, c: (c[r * slots + s], 0, 0))

    return pl.pallas_call(
        stiffness_kernel,
        out_shape=jax.ShapeDtypeStruct((blocks, rows, bs), jnp.bfloat16),
        grid_spec=pltpu.PrefetchScalarGridSpec(
            num_scalar_prefetch=1,
            grid=(blocks,),
            in_specs=[x_spec(s) for s in range(slots)]
            + [pl.BlockSpec((None, None, slots, bs, bs), lambda r, c: (term, r, 0, 0, 0))],
            out_specs=pl.BlockSpec((None, rows, bs), lambda r, c: (r, 0, 0)),
        ),
        cost_estimate=pl.CostEstimate(
            flops=2 * blocks * slots * rows * bs * bs,
            transcendentals=0,
            bytes_accessed=2 * (blocks * slots * bs * bs + blocks * slots * rows * bs + blocks * rows * bs),
        ),
    )(cols, ext, ext, ext, tiles_t)


def body(iterate, forcing, tiles, inverse_blocks, columns, coupling):
    modes_here, loads, dofs_here = iterate.shape
    terms, block_count, slots = tiles.shape[:3]
    block_size = dofs_here // block_count
    nm = lax.axis_size("mode")
    me = lax.axis_index("mode")
    cols = columns.reshape(-1).astype(jnp.int32)
    rounded = iterate.astype(jnp.bfloat16).reshape(modes_here, loads, block_count, block_size)
    own = jnp.transpose(rounded, (2, 0, 1, 3)).reshape(block_count, modes_here * loads, block_size)
    ext = jnp.concatenate(
        [shift(own[block_count - H:], "space", 1), own, shift(own[:H], "space", -1)], axis=0
    )
    coupling4 = coupling.reshape(terms, nm * modes_here, nm, modes_here)
    mixture = None
    for k in range(terms):
        tiles_k = jnp.swapaxes(
            tiles[k].reshape(1, block_count, slots, block_size, block_size), 3, 4
        )
        products = stiffness(cols, ext, tiles_k, 0)
        quarter = lax.all_to_all(products, "mode", 0, 0, tiled=True)
        quarter = quarter.reshape(nm, modes_here, loads, block_size)
        term = jnp.einsum(
            "aSp,Spli->ali",
            coupling4[k],
            quarter.astype(jnp.float32),
            precision=lax.Precision.HIGHEST,
        )
        mixture = term if mixture is None else mixture + term
    back = lax.all_to_all(mixture, "mode", 0, 0, tiled=True)
    back = back.reshape(nm, modes_here, loads, block_size)
    applied = jnp.transpose(back, (1, 2, 0, 3)).reshape(modes_here, loads, dofs_here)
    residual = forcing - applied
    rounded_res = residual.astype(jnp.bfloat16).reshape(modes_here, loads, block_count, block_size)
    inverse = inverse_blocks.reshape(block_count, block_size, block_size)
    update = jnp.einsum("jim,pljm->plji", inverse, rounded_res, preferred_element_type=jnp.float32)
    updated = iterate + RELAXATION * update.reshape(modes_here, loads, dofs_here)
    return (updated, residual)


def solution(mesh):
    return jax.shard_map(
        body,
        mesh=mesh,
        in_specs=(
            P("mode", None, "space"),
            P("mode", None, "space"),
            P(None, "space", None, None),
            P("space", None),
            P("space", None),
            P(),
        ),
        out_specs=(P("mode", None, "space"), P("mode", None, "space")),
        check_vma=False,
    )
```

```python
import jax
import jax.numpy as jnp
from jax import lax
from jax.sharding import PartitionSpec as P

H = 2


RELAXATION = 0.7


def padded(x, sides, width):
    for axis, dim in sides:
        devices, length = (lax.axis_size(axis), x.shape[dim])
        up = [(i, (i + 1) % devices) for i in range(devices)]
        down = [(j, i) for i, j in up]
        last = lax.slice_in_dim(x, length - width, length, axis=dim)
        initial = lax.slice_in_dim(x, 0, width, axis=dim)
        before = lax.ppermute(last, axis, up)
        after = lax.ppermute(initial, axis, down)
        x = jnp.concatenate([before, x, after], axis=dim)
    return x


def body(iterate, forcing, tiles, inverse_blocks, columns, coupling):
    modes_here, loads, dofs_here = iterate.shape
    terms, block_count, slots = tiles.shape[:3]
    block_size = dofs_here // block_count
    nm = lax.axis_size("mode")
    rounded = iterate.astype(jnp.bfloat16).reshape(modes_here, loads, block_count, block_size)
    extended = padded(rounded, (("space", 2),), H)
    picked = jnp.take(extended, columns, axis=2)
    coupling4 = coupling.reshape(terms, nm * modes_here, nm, modes_here)
    mixture = None
    for k in range(terms):
        shaped = tiles[k].reshape(block_count, slots, block_size, block_size)
        products = jnp.einsum(
            "rsim,plrsm->rpli", shaped, picked, preferred_element_type=jnp.float32
        ).astype(jnp.bfloat16)
        quarter = lax.all_to_all(products, "mode", 0, 0, tiled=True)
        term = jnp.einsum(
            "aSp,Spli->ali",
            coupling4[k],
            quarter.astype(jnp.float32),
            precision=lax.Precision.HIGHEST,
        )
        mixture = term if mixture is None else mixture + term
    back = lax.all_to_all(mixture, "mode", 0, 0, tiled=True)
    back = back.reshape(nm, modes_here, loads, block_size)
    applied = jnp.transpose(back, (1, 2, 0, 3)).reshape(modes_here, loads, dofs_here)
    residual = forcing - applied
    rounded_res = residual.astype(jnp.bfloat16).reshape(modes_here * loads, dofs_here)
    inverse = inverse_blocks.reshape(block_count, block_size, block_size)
    diagonal = jnp.eye(block_count, dtype=inverse.dtype)
    spread = jnp.einsum("rim,rs->rmsi", inverse, diagonal).reshape(dofs_here, dofs_here)
    update = jnp.dot(rounded_res, spread, preferred_element_type=jnp.float32)
    updated = iterate + RELAXATION * update.reshape(modes_here, loads, dofs_here)
    return (updated, residual)


def solution(mesh):
    return jax.shard_map(
        body,
        mesh=mesh,
        in_specs=(
            P("mode", None, "space"),
            P("mode", None, "space"),
            P(None, "space", None, None),
            P("space", None),
            P("space", None),
            P(),
        ),
        out_specs=(P("mode", None, "space"), P("mode", None, "space")),
        check_vma=False,
    )
```

```python
import jax
import jax.numpy as jnp
from jax import lax
from jax.sharding import PartitionSpec as P

H = 2


RELAXATION = 0.7


def padded(x, sides, width):
    for axis, dim in sides:
        devices, length = (lax.axis_size(axis), x.shape[dim])
        up = [(i, (i + 1) % devices) for i in range(devices)]
        down = [(j, i) for i, j in up]
        last = lax.slice_in_dim(x, length - width, length, axis=dim)
        initial = lax.slice_in_dim(x, 0, width, axis=dim)
        before = lax.ppermute(last, axis, up)
        after = lax.ppermute(initial, axis, down)
        x = jnp.concatenate([before, x, after], axis=dim)
    return x


def stiffness(extended, tile_rows, column_rows):
    block_size = extended.shape[-1]
    picked = jnp.take(extended, column_rows, axis=2)
    shaped = tile_rows.reshape(
        tile_rows.shape[0], tile_rows.shape[1], tile_rows.shape[2], block_size, block_size
    )
    return jnp.einsum("krsim,plrsm->kplri", shaped, picked, preferred_element_type=jnp.float32)


def body(iterate, forcing, tiles, inverse_blocks, columns, coupling):
    modes_here, loads, dofs_here = iterate.shape
    terms, block_count = (tiles.shape[0], tiles.shape[1])
    block_size = dofs_here // block_count
    rounded = iterate.astype(jnp.bfloat16).reshape(modes_here, loads, block_count, block_size)
    extended = padded(rounded, (("space", 2),), H)
    products = stiffness(extended, tiles, columns).astype(jnp.bfloat16)
    mixture = jnp.einsum(
        "kab,kblqn->alqn",
        coupling,
        lax.all_to_all(products, "mode", split_axis=3, concat_axis=1, tiled=True).astype(
            jnp.float32
        ),
        precision=lax.Precision.HIGHEST,
    )
    applied = lax.all_to_all(mixture, "mode", split_axis=0, concat_axis=2, tiled=True)
    applied = applied.reshape(modes_here, loads, dofs_here)
    residual = forcing - applied
    rounded_res = residual.astype(jnp.bfloat16).reshape(modes_here * loads, dofs_here)
    inverse = inverse_blocks.reshape(block_count, block_size, block_size)
    diagonal = jnp.eye(block_count, dtype=inverse.dtype)
    spread = jnp.einsum("rim,rs->rmsi", inverse, diagonal).reshape(dofs_here, dofs_here)
    update = jnp.dot(rounded_res, spread, preferred_element_type=jnp.float32)
    updated = iterate + RELAXATION * update.reshape(modes_here, loads, dofs_here)
    return (updated, residual)


def solution(mesh):
    return jax.shard_map(
        body,
        mesh=mesh,
        in_specs=(
            P("mode", None, "space"),
            P("mode", None, "space"),
            P(None, "space", None, None),
            P("space", None),
            P("space", None),
            P(),
        ),
        out_specs=(P("mode", None, "space"), P("mode", None, "space")),
        check_vma=False,
    )
```

```python
import jax
import jax.numpy as jnp
from jax import lax
from jax.sharding import PartitionSpec as P

H = 2


RELAXATION = 0.7


def halos(x, dim, width):
    lo = lax.axis_index("s_lo")
    length = x.shape[dim]
    last = lax.slice_in_dim(x, length - width, length, axis=dim)
    initial = lax.slice_in_dim(x, 0, width, axis=dim)
    inside = lax.ppermute(jnp.where(lo == 0, last, initial), "s_lo", [(0, 1), (1, 0)])
    chips = lax.axis_size("s_hi")
    pairs = []
    for c in range(chips):
        a, b = 2 * c + 1, 2 * ((c + 1) % chips)
        pairs += [(a, b), (b, a)]
    across = lax.ppermute(jnp.where(lo == 1, last, initial), ("s_hi", "s_lo"), pairs)
    before = jnp.where(lo == 0, across, inside)
    after = jnp.where(lo == 0, inside, across)
    return jnp.concatenate([before, x, after], axis=dim)


def stiffness(extended, tile_rows, column_rows):
    block_size = extended.shape[-1]
    picked = jnp.take(extended, column_rows, axis=2)
    shaped = tile_rows.reshape(
        tile_rows.shape[0], tile_rows.shape[1], tile_rows.shape[2], block_size, block_size
    )
    return jnp.einsum("krsim,plrsm->kplri", shaped, picked, preferred_element_type=jnp.float32)


def body(iterate, forcing, tiles, inverse_blocks, columns, coupling):
    modes_here, loads, dofs_here = iterate.shape
    terms, block_count = (tiles.shape[0], tiles.shape[1])
    block_size = dofs_here // block_count
    rounded = iterate.astype(jnp.bfloat16).reshape(modes_here, loads, block_count, block_size)
    extended = halos(rounded, 2, H)
    products = stiffness(extended, tiles, columns).astype(jnp.bfloat16)
    mixture = jnp.einsum(
        "kab,kblqn->alqn",
        coupling,
        lax.all_to_all(products, "mode", split_axis=3, concat_axis=1, tiled=True).astype(
            jnp.float32
        ),
        precision=lax.Precision.HIGHEST,
    )
    applied = lax.all_to_all(mixture, "mode", split_axis=0, concat_axis=2, tiled=True)
    applied = applied.reshape(modes_here, loads, dofs_here)
    residual = forcing - applied
    rounded_res = residual.astype(jnp.bfloat16).reshape(modes_here * loads, dofs_here)
    inverse = inverse_blocks.reshape(block_count, block_size, block_size)
    diagonal = jnp.eye(block_count, dtype=inverse.dtype)
    spread = jnp.einsum("rim,rs->rmsi", inverse, diagonal).reshape(dofs_here, dofs_here)
    update = jnp.dot(rounded_res, spread, preferred_element_type=jnp.float32)
    updated = iterate + RELAXATION * update.reshape(modes_here, loads, dofs_here)
    return (updated, residual)


def solution(mesh):
    space = mesh.shape["space"]
    pairs = jax.sharding.Mesh(
        mesh.devices.reshape(space // 2, 2, mesh.shape["mode"]), ("s_hi", "s_lo", "mode")
    )
    return jax.shard_map(
        body,
        mesh=pairs,
        in_specs=(
            P("mode", None, ("s_hi", "s_lo")),
            P("mode", None, ("s_hi", "s_lo")),
            P(None, ("s_hi", "s_lo"), None, None),
            P(("s_hi", "s_lo"), None),
            P(("s_hi", "s_lo"), None),
            P(),
        ),
        out_specs=(P("mode", None, ("s_hi", "s_lo")), P("mode", None, ("s_hi", "s_lo"))),
        check_vma=False,
    )
```

```python
import jax
import jax.numpy as jnp
from jax import lax
from jax.sharding import PartitionSpec as P

H = 2


RELAXATION = 0.7


def padded(x, sides, width, source):
    for axis, dim in sides:
        devices, length = (lax.axis_size(axis), x.shape[dim])
        up = [(i, (i + 1) % devices) for i in range(devices)]
        down = [(j, i) for i, j in up]
        dofs = source.shape[-1]
        edge = width * x.shape[-1]
        shape = x.shape[:dim] + (width,) + x.shape[dim + 1:]
        last = source[..., dofs - edge:].astype(x.dtype).reshape(shape)
        initial = source[..., :edge].astype(x.dtype).reshape(shape)
        before = lax.ppermute(last, axis, up)
        after = lax.ppermute(initial, axis, down)
        x = jnp.concatenate([before, x, after], axis=dim)
    return x


def stiffness(extended, tile_rows, column_rows):
    block_size = extended.shape[-1]
    picked = jnp.take(extended, column_rows, axis=2)
    shaped = tile_rows.reshape(
        tile_rows.shape[0], tile_rows.shape[1], tile_rows.shape[2], block_size, block_size
    )
    return jnp.einsum("krsim,plrsm->kplri", shaped, picked, preferred_element_type=jnp.float32)


def body(iterate, forcing, tiles, inverse_blocks, columns, coupling):
    modes_here, loads, dofs_here = iterate.shape
    terms, block_count = (tiles.shape[0], tiles.shape[1])
    block_size = dofs_here // block_count
    rounded = iterate.astype(jnp.bfloat16).reshape(modes_here, loads, block_count, block_size)
    extended = padded(rounded, (("space", 2),), H, iterate)
    products = stiffness(extended, tiles, columns).astype(jnp.bfloat16)
    exchanged = lax.all_to_all(products, "mode", split_axis=3, concat_axis=1, tiled=True)
    high = coupling.astype(jnp.bfloat16)
    rest = coupling - high.astype(jnp.float32)
    middle = rest.astype(jnp.bfloat16)
    low = (rest - middle.astype(jnp.float32)).astype(jnp.bfloat16)
    mixture = sum(
        jnp.einsum("kab,kblqn->alqn", piece, exchanged, preferred_element_type=jnp.float32)
        for piece in (high, middle, low)
    )
    applied = lax.all_to_all(mixture, "mode", split_axis=0, concat_axis=2, tiled=True)
    applied = applied.reshape(modes_here, loads, dofs_here)
    residual = forcing - applied
    rounded_res = residual.astype(jnp.bfloat16).reshape(modes_here * loads, dofs_here)
    inverse = inverse_blocks.reshape(block_count, block_size, block_size)
    diagonal = jnp.eye(block_count, dtype=inverse.dtype)
    spread = jnp.einsum("rim,rs->rmsi", inverse, diagonal).reshape(dofs_here, dofs_here)
    update = jnp.dot(rounded_res, spread, preferred_element_type=jnp.float32)
    updated = iterate + RELAXATION * update.reshape(modes_here, loads, dofs_here)
    return (updated, residual)


def solution(mesh):
    return jax.shard_map(
        body,
        mesh=mesh,
        in_specs=(
            P("mode", None, "space"),
            P("mode", None, "space"),
            P(None, "space", None, None),
            P("space", None),
            P("space", None),
            P(),
        ),
        out_specs=(P("mode", None, "space"), P("mode", None, "space")),
        check_vma=False,
    )
```

```python
import jax
import jax.numpy as jnp
from jax import lax
from jax.sharding import PartitionSpec as P

H = 2


RELAXATION = 0.7


def padded(x, sides, width, source):
    for axis, dim in sides:
        devices, length = (lax.axis_size(axis), x.shape[dim])
        up = [(i, (i + 1) % devices) for i in range(devices)]
        down = [(j, i) for i, j in up]
        dofs = source.shape[-1]
        edge = width * x.shape[-1]
        shape = x.shape[:dim] + (width,) + x.shape[dim + 1:]
        last = source[..., dofs - edge:].astype(x.dtype).reshape(shape)
        initial = source[..., :edge].astype(x.dtype).reshape(shape)
        before = lax.ppermute(last, axis, up)
        after = lax.ppermute(initial, axis, down)
        x = jnp.concatenate([before, x, after], axis=dim)
    return x


def stiffness(extended, tile_rows, column_rows):
    block_size = extended.shape[-1]
    picked = jnp.take(extended, column_rows, axis=2)
    shaped = tile_rows.reshape(
        tile_rows.shape[0], tile_rows.shape[1], tile_rows.shape[2], block_size, block_size
    )
    return jnp.einsum("krsim,plrsm->kplri", shaped, picked, preferred_element_type=jnp.float32)


def body(iterate, forcing, tiles, inverse_blocks, columns, coupling):
    modes_here, loads, dofs_here = iterate.shape
    terms, block_count = (tiles.shape[0], tiles.shape[1])
    block_size = dofs_here // block_count
    rounded = iterate.astype(jnp.bfloat16).reshape(modes_here, loads, block_count, block_size)
    extended = padded(rounded, (("space", 2),), H, iterate)
    products = stiffness(extended, tiles, columns).astype(jnp.bfloat16)
    exchanged = lax.all_to_all(products, "mode", split_axis=3, concat_axis=1, tiled=True)
    high = lax.reduce_precision(coupling, exponent_bits=8, mantissa_bits=7)
    rest = coupling - high
    middle = lax.reduce_precision(rest, exponent_bits=8, mantissa_bits=7)
    low = rest - middle
    mixture = sum(
        jnp.einsum(
            "kab,kblqn->alqn",
            piece.astype(jnp.bfloat16),
            exchanged,
            preferred_element_type=jnp.float32,
        )
        for piece in (high, middle, low)
    )
    applied = lax.all_to_all(mixture, "mode", split_axis=0, concat_axis=2, tiled=True)
    applied = applied.reshape(modes_here, loads, dofs_here)
    residual = forcing - applied
    rounded_res = residual.astype(jnp.bfloat16).reshape(modes_here * loads, dofs_here)
    inverse = inverse_blocks.reshape(block_count, block_size, block_size)
    diagonal = jnp.eye(block_count, dtype=inverse.dtype)
    spread = jnp.einsum("rim,rs->rmsi", inverse, diagonal).reshape(dofs_here, dofs_here)
    update = jnp.dot(rounded_res, spread, preferred_element_type=jnp.float32)
    updated = iterate + RELAXATION * update.reshape(modes_here, loads, dofs_here)
    return (updated, residual)


def solution(mesh):
    return jax.shard_map(
        body,
        mesh=mesh,
        in_specs=(
            P("mode", None, "space"),
            P("mode", None, "space"),
            P(None, "space", None, None),
            P("space", None),
            P("space", None),
            P(),
        ),
        out_specs=(P("mode", None, "space"), P("mode", None, "space")),
        check_vma=False,
    )
```

```python
import jax
import jax.numpy as jnp
from jax import lax
from jax.sharding import PartitionSpec as P

H = 2


RELAXATION = 0.7


def padded(x, sides, width, cover):
    for axis, dim in sides:
        devices, length = (lax.axis_size(axis), x.shape[dim])
        up = [(i, (i + 1) % devices) for i in range(devices)]
        down = [(j, i) for i, j in up]
        last = lax.slice_in_dim(x, length - width, length, axis=dim)
        initial = lax.slice_in_dim(x, 0, width, axis=dim)
        before = lax.ppermute(last, axis, up)
        before, initial = lax.optimization_barrier((before, initial))
        initial, covered = lax.optimization_barrier((initial, cover(before)))
        after = lax.ppermute(initial, axis, down)
        x = jnp.concatenate([before, x, after], axis=dim)
    return x, covered


def stiffness(extended, shaped, column_rows):
    picked = jnp.take(extended, column_rows, axis=2)
    return jnp.einsum("krsim,plrsm->kplri", shaped, picked, preferred_element_type=jnp.float32)


def body(iterate, forcing, tiles, inverse_blocks, columns, coupling):
    modes_here, loads, dofs_here = iterate.shape
    terms, block_count = (tiles.shape[0], tiles.shape[1])
    block_size = dofs_here // block_count
    rounded = iterate.astype(jnp.bfloat16).reshape(modes_here, loads, block_count, block_size)
    extended, shaped = padded(
        rounded,
        (("space", 2),),
        H,
        lambda ready: lax.optimization_barrier((ready, tiles))[1].reshape(
            terms, block_count, tiles.shape[2], block_size, block_size
        ),
    )
    products = stiffness(extended, shaped, columns).astype(jnp.bfloat16)
    mixture = jnp.einsum(
        "kab,kblqn->alqn",
        coupling,
        lax.all_to_all(products, "mode", split_axis=3, concat_axis=1, tiled=True).astype(
            jnp.float32
        ),
        precision=lax.Precision.HIGHEST,
    )
    applied = lax.all_to_all(mixture, "mode", split_axis=0, concat_axis=2, tiled=True)
    applied = applied.reshape(modes_here, loads, dofs_here)
    residual = forcing - applied
    rounded_res = residual.astype(jnp.bfloat16).reshape(modes_here * loads, dofs_here)
    inverse = inverse_blocks.reshape(block_count, block_size, block_size)
    diagonal = jnp.eye(block_count, dtype=inverse.dtype)
    spread = jnp.einsum("rim,rs->rmsi", inverse, diagonal).reshape(dofs_here, dofs_here)
    update = jnp.dot(rounded_res, spread, preferred_element_type=jnp.float32)
    updated = iterate + RELAXATION * update.reshape(modes_here, loads, dofs_here)
    return (updated, residual)


def solution(mesh):
    return jax.shard_map(
        body,
        mesh=mesh,
        in_specs=(
            P("mode", None, "space"),
            P("mode", None, "space"),
            P(None, "space", None, None),
            P("space", None),
            P("space", None),
            P(),
        ),
        out_specs=(P("mode", None, "space"), P("mode", None, "space")),
        check_vma=False,
    )
```

```python
import jax
import jax.numpy as jnp
from jax import lax
from jax.sharding import PartitionSpec as P

H = 2


RELAXATION = 0.7


def padded(x, sides, width):
    for axis, dim in sides:
        devices, length = (lax.axis_size(axis), x.shape[dim])
        up = [(i, (i + 1) % devices) for i in range(devices)]
        down = [(j, i) for i, j in up]
        last = lax.slice_in_dim(x, length - width, length, axis=dim)
        initial = lax.slice_in_dim(x, 0, width, axis=dim)
        before = lax.ppermute(last, axis, up)
        after = lax.ppermute(initial, axis, down)
        x = jnp.concatenate([before, x, after], axis=dim)
    return x


def pick(extended, column_rows, width):
    blocks = column_rows.shape[0]
    rows = []
    for r in range(blocks):
        near = width + r
        chosen = [extended[:, :, near]]
        for s, options in ((1, (near - 2, near - 1)), (2, (near + 2, near + 1))):
            if (s == 1 and r == 0) or (s == 2 and r == blocks - 1):
                chosen.append(extended[:, :, options[0]])
            else:
                chosen.append(
                    jnp.where(
                        column_rows[r, s] == options[0],
                        extended[:, :, options[0]],
                        extended[:, :, options[1]],
                    )
                )
        rows.append(jnp.stack(chosen, axis=2))
    return jnp.stack(rows, axis=2)


def stiffness(extended, tile_rows, column_rows):
    block_size = extended.shape[-1]
    picked = pick(extended, column_rows, H)
    shaped = tile_rows.reshape(
        tile_rows.shape[0], tile_rows.shape[1], tile_rows.shape[2], block_size, block_size
    )
    return jnp.einsum("krsim,plrsm->kplri", shaped, picked, preferred_element_type=jnp.float32)


def body(iterate, forcing, tiles, inverse_blocks, columns, coupling):
    modes_here, loads, dofs_here = iterate.shape
    terms, block_count = (tiles.shape[0], tiles.shape[1])
    block_size = dofs_here // block_count
    rounded = iterate.astype(jnp.bfloat16).reshape(modes_here, loads, block_count, block_size)
    extended = padded(rounded, (("space", 2),), H)
    products = stiffness(extended, tiles, columns).astype(jnp.bfloat16)
    mixture = jnp.einsum(
        "kab,kblqn->alqn",
        coupling,
        lax.all_to_all(products, "mode", split_axis=3, concat_axis=1, tiled=True).astype(
            jnp.float32
        ),
        precision=lax.Precision.HIGHEST,
    )
    applied = lax.all_to_all(mixture, "mode", split_axis=0, concat_axis=2, tiled=True)
    applied = applied.reshape(modes_here, loads, dofs_here)
    residual = forcing - applied
    rounded_res = residual.astype(jnp.bfloat16).reshape(modes_here * loads, dofs_here)
    inverse = inverse_blocks.reshape(block_count, block_size, block_size)
    diagonal = jnp.eye(block_count, dtype=inverse.dtype)
    spread = jnp.einsum("rim,rs->rmsi", inverse, diagonal).reshape(dofs_here, dofs_here)
    update = jnp.dot(rounded_res, spread, preferred_element_type=jnp.float32)
    updated = iterate + RELAXATION * update.reshape(modes_here, loads, dofs_here)
    return (updated, residual)


def solution(mesh):
    return jax.shard_map(
        body,
        mesh=mesh,
        in_specs=(
            P("mode", None, "space"),
            P("mode", None, "space"),
            P(None, "space", None, None),
            P("space", None),
            P("space", None),
            P(),
        ),
        out_specs=(P("mode", None, "space"), P("mode", None, "space")),
        check_vma=False,
    )
```

```python
import jax
import jax.numpy as jnp
from jax import lax
from jax.sharding import PartitionSpec as P

H = 2


RELAXATION = 0.7


def padded(x, sides, width):
    for axis, dim in sides:
        devices, length = (lax.axis_size(axis), x.shape[dim])
        up = [(i, (i + 1) % devices) for i in range(devices)]
        down = [(j, i) for i, j in up]
        last = lax.slice_in_dim(x, length - width, length, axis=dim)
        initial = lax.slice_in_dim(x, 0, width, axis=dim)
        before = lax.ppermute(last, axis, up)
        after = lax.ppermute(initial, axis, down)
        x = jnp.concatenate([before, x, after], axis=dim)
    return x


def stiffness(extended, tile_rows, column_rows):
    block_size = extended.shape[-1]
    picked = jnp.take(extended, column_rows, axis=2)
    shaped = tile_rows.reshape(
        tile_rows.shape[0], tile_rows.shape[1], tile_rows.shape[2], block_size, block_size
    )
    return jnp.einsum("krsim,plrsm->kplri", shaped, picked, preferred_element_type=jnp.float32)


def body(iterate, forcing, tiles, inverse_blocks, columns, coupling):
    modes_here, loads, dofs_here = iterate.shape
    terms, block_count = (tiles.shape[0], tiles.shape[1])
    block_size = dofs_here // block_count
    rounded = iterate.astype(jnp.bfloat16).reshape(modes_here, loads, block_count, block_size)
    extended = padded(rounded, (("space", 2),), H)
    products = stiffness(extended, tiles, columns).astype(jnp.bfloat16)
    exchanged = lax.all_to_all(products, "mode", split_axis=3, concat_axis=1, tiled=True)
    high = lax.reduce_precision(coupling, exponent_bits=8, mantissa_bits=7)
    rest = coupling - high
    middle = lax.reduce_precision(rest, exponent_bits=8, mantissa_bits=7)
    pieces = jnp.stack([high, middle, rest - middle]).astype(jnp.bfloat16)
    mixture = jnp.einsum(
        "jkab,kblqn->jalqn", pieces, exchanged, preferred_element_type=jnp.float32
    ).sum(axis=0)
    applied = lax.all_to_all(mixture, "mode", split_axis=0, concat_axis=2, tiled=True)
    applied = applied.reshape(modes_here, loads, dofs_here)
    residual = forcing - applied
    rounded_res = residual.astype(jnp.bfloat16).reshape(modes_here * loads, dofs_here)
    inverse = inverse_blocks.reshape(block_count, block_size, block_size)
    diagonal = jnp.eye(block_count, dtype=inverse.dtype)
    spread = jnp.einsum("rim,rs->rmsi", inverse, diagonal).reshape(dofs_here, dofs_here)
    update = jnp.dot(rounded_res, spread, preferred_element_type=jnp.float32)
    updated = iterate + RELAXATION * update.reshape(modes_here, loads, dofs_here)
    return (updated, residual)


def solution(mesh):
    return jax.shard_map(
        body,
        mesh=mesh,
        in_specs=(
            P("mode", None, "space"),
            P("mode", None, "space"),
            P(None, "space", None, None),
            P("space", None),
            P("space", None),
            P(),
        ),
        out_specs=(P("mode", None, "space"), P("mode", None, "space")),
        check_vma=False,
    )
```

```python
import jax
import jax.numpy as jnp
from jax import lax
from jax.sharding import PartitionSpec as P

H = 2


RELAXATION = 0.7


def padded(x, sides, width):
    for axis, dim in sides:
        devices, length = (lax.axis_size(axis), x.shape[dim])
        up = [(i, (i + 1) % devices) for i in range(devices)]
        down = [(j, i) for i, j in up]
        last = lax.slice_in_dim(x, length - width, length, axis=dim)
        initial = lax.slice_in_dim(x, 0, width, axis=dim)
        before = lax.ppermute(last, axis, up)
        after = lax.ppermute(initial, axis, down)
        x = jnp.concatenate([before, x, after], axis=dim)
    return x


def stiffness(extended, tile_rows, column_rows):
    block_size = extended.shape[-1]
    picked = jnp.take(extended, column_rows, axis=2, mode="clip")
    shaped = tile_rows.reshape(
        tile_rows.shape[0], tile_rows.shape[1], tile_rows.shape[2], block_size, block_size
    )
    return jnp.einsum("krsim,plrsm->kplri", shaped, picked, preferred_element_type=jnp.float32)


def body(iterate, forcing, tiles, inverse_blocks, columns, coupling):
    modes_here, loads, dofs_here = iterate.shape
    terms, block_count = (tiles.shape[0], tiles.shape[1])
    block_size = dofs_here // block_count
    rounded = iterate.astype(jnp.bfloat16).reshape(modes_here, loads, block_count, block_size)
    extended = padded(rounded, (("space", 2),), H)
    products = stiffness(extended, tiles, columns).astype(jnp.bfloat16)
    exchanged = lax.all_to_all(products, "mode", split_axis=3, concat_axis=1, tiled=True)
    high = lax.reduce_precision(coupling, exponent_bits=8, mantissa_bits=7)
    rest = coupling - high
    middle = lax.reduce_precision(rest, exponent_bits=8, mantissa_bits=7)
    pieces = jnp.stack([high, middle, rest - middle]).astype(jnp.bfloat16)
    mixture = jnp.einsum(
        "jkab,kblqn->jalqn", pieces, exchanged, preferred_element_type=jnp.float32
    ).sum(axis=0)
    applied = lax.all_to_all(mixture, "mode", split_axis=0, concat_axis=2, tiled=True)
    applied = applied.reshape(modes_here, loads, dofs_here)
    residual = forcing - applied
    rounded_res = residual.astype(jnp.bfloat16).reshape(modes_here * loads, dofs_here)
    inverse = inverse_blocks.reshape(block_count, block_size, block_size)
    diagonal = jnp.eye(block_count, dtype=inverse.dtype)
    spread = jnp.einsum("rim,rs->rmsi", inverse, diagonal).reshape(dofs_here, dofs_here)
    update = jnp.dot(rounded_res, spread, preferred_element_type=jnp.float32)
    updated = iterate + RELAXATION * update.reshape(modes_here, loads, dofs_here)
    return (updated, residual)


def solution(mesh):
    return jax.shard_map(
        body,
        mesh=mesh,
        in_specs=(
            P("mode", None, "space"),
            P("mode", None, "space"),
            P(None, "space", None, None),
            P("space", None),
            P("space", None),
            P(),
        ),
        out_specs=(P("mode", None, "space"), P("mode", None, "space")),
        check_vma=False,
    )
```

```python
import jax
import jax.numpy as jnp
from jax import lax
from jax.sharding import PartitionSpec as P

H = 2


RELAXATION = 0.7


def padded(x, sides, width):
    for axis, dim in sides:
        devices, length = (lax.axis_size(axis), x.shape[dim])
        up = [(i, (i + 1) % devices) for i in range(devices)]
        down = [(j, i) for i, j in up]
        last = lax.slice_in_dim(x, length - width, length, axis=dim)
        initial = lax.slice_in_dim(x, 0, width, axis=dim)
        before = lax.ppermute(last, axis, up)
        after = lax.ppermute(initial, axis, down)
        x = jnp.concatenate([before, x, after], axis=dim)
    return x


def stiffness(extended, tile_rows, column_rows):
    block_size = extended.shape[-1]
    picked = jnp.take(extended, column_rows, axis=2)
    shaped = tile_rows.reshape(
        tile_rows.shape[0], tile_rows.shape[1], tile_rows.shape[2], block_size, block_size
    )
    return jnp.stack(
        [
            jnp.einsum(
                "ksim,plsm->kpli",
                shaped[:, r],
                picked[:, :, r],
                preferred_element_type=jnp.float32,
            )
            for r in range(shaped.shape[1])
        ],
        axis=3,
    )


def body(iterate, forcing, tiles, inverse_blocks, columns, coupling):
    modes_here, loads, dofs_here = iterate.shape
    terms, block_count = (tiles.shape[0], tiles.shape[1])
    block_size = dofs_here // block_count
    rounded = iterate.astype(jnp.bfloat16).reshape(modes_here, loads, block_count, block_size)
    extended = padded(rounded, (("space", 2),), H)
    products = stiffness(extended, tiles, columns).astype(jnp.bfloat16)
    exchanged = lax.all_to_all(products, "mode", split_axis=3, concat_axis=1, tiled=True)
    high = lax.reduce_precision(coupling, exponent_bits=8, mantissa_bits=7)
    rest = coupling - high
    middle = lax.reduce_precision(rest, exponent_bits=8, mantissa_bits=7)
    pieces = jnp.stack([high, middle, rest - middle]).astype(jnp.bfloat16)
    mixture = jnp.einsum(
        "jkab,kblqn->jalqn", pieces, exchanged, preferred_element_type=jnp.float32
    ).sum(axis=0)
    applied = lax.all_to_all(mixture, "mode", split_axis=0, concat_axis=2, tiled=True)
    applied = applied.reshape(modes_here, loads, dofs_here)
    residual = forcing - applied
    rounded_res = residual.astype(jnp.bfloat16).reshape(modes_here * loads, dofs_here)
    inverse = inverse_blocks.reshape(block_count, block_size, block_size)
    diagonal = jnp.eye(block_count, dtype=inverse.dtype)
    spread = jnp.einsum("rim,rs->rmsi", inverse, diagonal).reshape(dofs_here, dofs_here)
    update = jnp.dot(rounded_res, spread, preferred_element_type=jnp.float32)
    updated = iterate + RELAXATION * update.reshape(modes_here, loads, dofs_here)
    return (updated, residual)


def solution(mesh):
    return jax.shard_map(
        body,
        mesh=mesh,
        in_specs=(
            P("mode", None, "space"),
            P("mode", None, "space"),
            P(None, "space", None, None),
            P("space", None),
            P("space", None),
            P(),
        ),
        out_specs=(P("mode", None, "space"), P("mode", None, "space")),
        check_vma=False,
    )
```

```python
import jax
import jax.numpy as jnp
from jax import lax
from jax.sharding import PartitionSpec as P

H = 2


RELAXATION = 0.7


def padded(x, sides, width):
    for axis, dim in sides:
        devices, length = (lax.axis_size(axis), x.shape[dim])
        up = [(i, (i + 1) % devices) for i in range(devices)]
        down = [(j, i) for i, j in up]
        last = lax.slice_in_dim(x, length - width, length, axis=dim)
        initial = lax.slice_in_dim(x, 0, width, axis=dim)
        before = lax.ppermute(last, axis, up)
        after = lax.ppermute(initial, axis, down)
        x = jnp.concatenate([before, x, after], axis=dim)
    return x


def stiffness(extended, tile_rows, column_rows):
    block_size = extended.shape[-1]
    picked = jnp.take(extended, column_rows, axis=2)
    shaped = tile_rows.reshape(
        tile_rows.shape[0], tile_rows.shape[1], tile_rows.shape[2], block_size, block_size
    )
    return jnp.stack(
        [
            jnp.einsum(
                "ksim,plsm->kpli",
                shaped[:, r],
                picked[:, :, r],
                preferred_element_type=jnp.float32,
            )
            for r in range(shaped.shape[1])
        ]
    )


def body(iterate, forcing, tiles, inverse_blocks, columns, coupling):
    modes_here, loads, dofs_here = iterate.shape
    terms, block_count = (tiles.shape[0], tiles.shape[1])
    block_size = dofs_here // block_count
    rounded = iterate.astype(jnp.bfloat16).reshape(modes_here, loads, block_count, block_size)
    extended = padded(rounded, (("space", 2),), H)
    products = stiffness(extended, tiles, columns).astype(jnp.bfloat16)
    exchanged = lax.all_to_all(products, "mode", split_axis=0, concat_axis=0, tiled=True)
    sources = lax.axis_size("mode")
    high = lax.reduce_precision(coupling, exponent_bits=8, mantissa_bits=7)
    rest = coupling - high
    middle = lax.reduce_precision(rest, exponent_bits=8, mantissa_bits=7)
    pieces = jnp.stack([high, middle, rest - middle]).astype(jnp.bfloat16)
    pieces = pieces.reshape(pieces.shape[:3] + (sources, modes_here))
    mixture = jnp.einsum(
        "jkaSp,Skpli->jali", pieces, exchanged, preferred_element_type=jnp.float32
    ).sum(axis=0)[:, :, None, :]
    applied = lax.all_to_all(mixture, "mode", split_axis=0, concat_axis=2, tiled=True)
    applied = applied.reshape(modes_here, loads, dofs_here)
    residual = forcing - applied
    rounded_res = residual.astype(jnp.bfloat16).reshape(modes_here * loads, dofs_here)
    inverse = inverse_blocks.reshape(block_count, block_size, block_size)
    diagonal = jnp.eye(block_count, dtype=inverse.dtype)
    spread = jnp.einsum("rim,rs->rmsi", inverse, diagonal).reshape(dofs_here, dofs_here)
    update = jnp.dot(rounded_res, spread, preferred_element_type=jnp.float32)
    updated = iterate + RELAXATION * update.reshape(modes_here, loads, dofs_here)
    return (updated, residual)


def solution(mesh):
    return jax.shard_map(
        body,
        mesh=mesh,
        in_specs=(
            P("mode", None, "space"),
            P("mode", None, "space"),
            P(None, "space", None, None),
            P("space", None),
            P("space", None),
            P(),
        ),
        out_specs=(P("mode", None, "space"), P("mode", None, "space")),
        check_vma=False,
    )
```

```python
import jax
import jax.numpy as jnp
from jax import lax
from jax.sharding import PartitionSpec as P

H = 2


RELAXATION = 0.7


def padded(x, sides, width, source):
    for axis, dim in sides:
        devices, length = (lax.axis_size(axis), x.shape[dim])
        up = [(i, (i + 1) % devices) for i in range(devices)]
        down = [(j, i) for i, j in up]
        dofs = source.shape[-1]
        edge = width * x.shape[-1]
        shape = x.shape[:dim] + (width,) + x.shape[dim + 1:]
        last = source[..., dofs - edge:].astype(x.dtype).reshape(shape)
        initial = source[..., :edge].astype(x.dtype).reshape(shape)
        before = lax.ppermute(last, axis, up)
        after = lax.ppermute(initial, axis, down)
        x = jnp.concatenate([before, x, after], axis=dim)
    return x


def stiffness(extended, tile_rows, column_rows):
    block_size = extended.shape[-1]
    picked = jnp.take(extended, column_rows, axis=2)
    shaped = tile_rows.reshape(
        tile_rows.shape[0], tile_rows.shape[1], tile_rows.shape[2], block_size, block_size
    )
    return jnp.einsum("krsim,plrsm->kplri", shaped, picked, preferred_element_type=jnp.float32)


def body(iterate, forcing, tiles, inverse_blocks, columns, coupling):
    modes_here, loads, dofs_here = iterate.shape
    terms, block_count = (tiles.shape[0], tiles.shape[1])
    block_size = dofs_here // block_count
    rounded = iterate.astype(jnp.bfloat16).reshape(modes_here, loads, block_count, block_size)
    extended = padded(rounded, (("space", 2),), H, iterate)
    products = stiffness(extended, tiles, columns).astype(jnp.bfloat16)
    exchanged = lax.all_to_all(products, "mode", split_axis=3, concat_axis=1, tiled=True)
    high = lax.reduce_precision(coupling, exponent_bits=8, mantissa_bits=7)
    rest = coupling - high
    middle = lax.reduce_precision(rest, exponent_bits=8, mantissa_bits=7)
    pieces = jnp.stack([high, middle, rest - middle]).astype(jnp.bfloat16)
    mixture = jnp.einsum(
        "jkab,kblqn->jalqn", pieces, exchanged, preferred_element_type=jnp.float32
    ).sum(axis=0)
    applied = lax.all_to_all(mixture, "mode", split_axis=0, concat_axis=2, tiled=True)
    applied = applied.reshape(modes_here, loads, dofs_here)
    residual = forcing - applied
    rounded_res = residual.astype(jnp.bfloat16).reshape(modes_here * loads, dofs_here)
    inverse = inverse_blocks.reshape(block_count, block_size, block_size)
    diagonal = jnp.eye(block_count, dtype=inverse.dtype)
    spread = jnp.einsum("rim,rs->rmsi", inverse, diagonal).reshape(dofs_here, dofs_here)
    update = jnp.dot(rounded_res, spread, preferred_element_type=jnp.float32)
    updated = iterate + RELAXATION * update.reshape(modes_here, loads, dofs_here)
    return (updated, residual)


def solution(mesh):
    return jax.shard_map(
        body,
        mesh=mesh,
        in_specs=(
            P("mode", None, "space"),
            P("mode", None, "space"),
            P(None, "space", None, None),
            P("space", None),
            P("space", None),
            P(),
        ),
        out_specs=(P("mode", None, "space"), P("mode", None, "space")),
        check_vma=False,
    )
```
